32 devices in a mesh: groups: 2 (over y), rows: 16 (over z, x, core).
Axes of the slice: x: 2, y: 2, z: 4, core: 2. Of those that a mesh axis runs over, the one named last changes fastest.
Arguments:
- queries: bfloat16 [32, 4096], P(('groups', 'rows')), parts along dimension 0, may hold values from -135 to 135
- keys: bfloat16 [32, 384, 512], P(('groups', 'rows')), parts along dimension 0, may hold values from -4.5 to 4.5
- values: bfloat16 [32, 384, 512], P(('groups', 'rows')), parts along dimension 0, may hold values from -4.5 to 4.5
- lengths: int32 [32], P(('groups', 'rows')), parts along dimension 0, may hold values from 2 to 384
- resid: bfloat16 [32, 4096], P(('groups', 'rows')), parts along dimension 0, may hold values from -6 to 6
- out_weight: bfloat16 [4096, 4096], P('rows'), may hold values from -0.09375 to 0.09375
- chat_ids: int32 [256], replicated, may hold values from 0 to 8191, as said below
- enc_weight: bfloat16 [4096, 8192], P(None, 'rows'), may hold values from -0.09375 to 0.09375
- enc_bias: float32 [8192], P('rows'), may hold values from -3 to 3
- dec_weight: bfloat16 [8192, 4096], P('rows'), may hold values from -0.09375 to 0.09375
- dec_bias: float32 [4096], replicated, may hold values from -3 to 3
Outputs:
- spliced: bfloat16 [32, 4096], P(('groups', 'rows')), parts along dimension 0
- activity: bfloat16 [32, 8192], P('groups', 'rows'), parts along dimension 0
The draws below stay inside these ranges and needn't reach their ends.
There are 2 independent parts, one for each index of `groups`. The reference program is written for one: setup_inputs(seed, part) draws one part's arguments, and reference() takes and returns one part's arrays. A program takes and returns all parts, laid end to end along the dimension named above; an argument that names none is the same for every part. Nothing has to cross between parts.
Inputs may be any that keep to these rules, and one draw needn't show every extreme that they name: `chat_ids`: 256 distinct latent numbers.
All inputs are finite; a program needn't handle non-finite values.
Results may differ from the reference program's by a relative error of at most 0.0057.
Values may be sent and summed in bfloat16 or wider, within the bound.
No kernel may reach another device: no remote copies, remote signals or barrier semaphores. Data moves between devices by JAX's collectives and lax.ppermute only.
A program may use at most 64 MiB of HBM per device.

```python
import jax
import jax.numpy as jnp
from jax import lax

D = 4096
HEADS = 32
KV_HEADS = 4
HEAD_DIM = 128
KV_MAX = 384
ROWS = 16
LATENTS = 8192
NCHAT = 256


def shared_keys(key):
    base = jnp.clip(jax.random.normal(jax.random.fold_in(key, 11), (ROWS, KV_MAX, KV_HEADS * HEAD_DIM), jnp.float32), -4.5, 4.5)
    return base


def draw_keys(key, part):
    return shared_keys(key).astype(jnp.bfloat16)


def draw_queries(key, part):
    drawn = jnp.clip(jax.random.normal(jax.random.fold_in(key, 23), (ROWS, HEADS * HEAD_DIM), jnp.float32), -4.5, 4.5)
    return drawn.astype(jnp.bfloat16)


def draw_lengths(key, part):
    first = jax.random.randint(jax.random.fold_in(key, 31), (ROWS,), 0, KV_MAX)
    second = jax.random.randint(jax.random.fold_in(key, 32), (ROWS,), 0, KV_MAX)
    raw = 2 + first * second // KV_MAX
    picked = jax.random.randint(jax.random.fold_in(key, 33), (), 0, ROWS)
    row_number = jnp.arange(ROWS)
    raw = jnp.where(row_number == picked, KV_MAX, raw)
    raw = jnp.where(row_number == (picked + 1) % ROWS, 2, raw)
    return raw.astype(jnp.int32)


def draw_chat_ids(key, part):
    inner = jax.random.permutation(jax.random.fold_in(key, 41), LATENTS - 2)[:NCHAT - 2] + 1
    whole = jnp.concatenate([jnp.array([0, LATENTS - 1], jnp.int32), inner.astype(jnp.int32)])
    return jax.random.permutation(jax.random.fold_in(key, 42), whole).astype(jnp.int32)


def shard_levels(key, extent, split, smallest, largest):
    def one(axis_at, blocks):
        draws = jax.random.uniform(jax.random.fold_in(jax.random.fold_in(key, 6), axis_at), (blocks,), jnp.float32, smallest / len(split), largest / len(split))
        return jnp.repeat(jnp.exp(draws), extent[axis_at] // blocks).reshape((-1,) + (1,) * (len(extent) - axis_at - 1))

    factor_of = one(*split[0])
    for cut in split[1:]:
        factor_of = factor_of * one(*cut)
    return factor_of


def gaussian(rng, extent, deviation, reach, pieces=(), kind=jnp.bfloat16):
    entries = deviation * jax.random.normal(rng, extent, jnp.float32)
    if pieces:
        entries = entries * shard_levels(rng, extent, pieces, -0.22, 0.18)
    return jnp.clip(entries, -reach, reach).astype(kind)


def setup_inputs(seed: int = 0, part: int = 0) -> dict:
    streams_of = jax.random.split(jax.random.key(seed), 12)
    part_keys = jax.random.split(jax.random.fold_in(streams_of[11], part), 12)
    queries = draw_queries(jax.random.fold_in(jax.random.fold_in(streams_of[11], part), 71), part)
    keys = draw_keys(jax.random.fold_in(jax.random.fold_in(streams_of[11], part), 71), part)
    values = gaussian(part_keys[2], (ROWS, KV_MAX, KV_HEADS * HEAD_DIM), 1.0, 4.5, ((0, 16),))
    lengths = draw_lengths(jax.random.fold_in(jax.random.fold_in(streams_of[11], part), 71), part)
    resid = gaussian(part_keys[4], (ROWS, D), 1.0, 6.0, ((0, 16),))
    out_weight = gaussian(streams_of[5], (HEADS * HEAD_DIM, D), (HEADS * HEAD_DIM) ** -0.5, 0.09375, ((0, 16),))
    chat_ids = draw_chat_ids(jax.random.fold_in(streams_of[11], 71), part)
    enc_weight = gaussian(streams_of[7], (D, LATENTS), D ** -0.5, 0.09375, ((1, 16),))
    enc_bias = gaussian(streams_of[8], (LATENTS,), 0.5, 3.0, ((0, 16),), jnp.float32)
    dec_weight = gaussian(streams_of[9], (LATENTS, D), (LATENTS // 2) ** -0.5, 0.09375, ((0, 16),))
    dec_bias = gaussian(streams_of[10], (D,), 0.5, 3.0, (), jnp.float32)
    return {"queries": queries, "keys": keys, "values": values, "lengths": lengths, "resid": resid, "out_weight": out_weight, "chat_ids": chat_ids, "enc_weight": enc_weight, "enc_bias": enc_bias, "dec_weight": dec_weight, "dec_bias": dec_bias}


def reference(queries, keys, values, lengths, resid, out_weight, chat_ids, enc_weight, enc_bias, dec_weight, dec_bias):
    group_size = HEADS // KV_HEADS
    query_heads = queries.astype(jnp.float32).reshape(ROWS, KV_HEADS, group_size, HEAD_DIM)
    key_heads = keys.astype(jnp.float32).reshape(ROWS, KV_MAX, KV_HEADS, HEAD_DIM)
    value_heads = values.astype(jnp.float32).reshape(ROWS, KV_MAX, KV_HEADS, HEAD_DIM)
    scores = jnp.einsum('rkgd,rskd->rkgs', query_heads, key_heads) / jnp.sqrt(jnp.float32(HEAD_DIM))
    visible = jnp.arange(KV_MAX, dtype=jnp.int32)[None, :] < lengths[:, None]
    scores = jnp.where(visible[:, None, None, :], scores, -jnp.inf)
    highest = lax.optimization_barrier(jnp.max(scores, axis=-1, keepdims=True))
    expo = jnp.exp(scores - highest)
    weights = (expo / lax.optimization_barrier(jnp.sum(expo, axis=-1, keepdims=True))).astype(jnp.bfloat16)
    attended = jnp.einsum('rkgs,rskd->rkgd', weights.astype(jnp.float32), value_heads)
    attended = attended.astype(jnp.bfloat16).reshape(ROWS, HEADS * HEAD_DIM)
    hidden = (resid.astype(jnp.float32) + jnp.dot(attended, out_weight, preferred_element_type=jnp.float32)).astype(jnp.bfloat16)
    pre = jnp.dot(hidden, enc_weight, preferred_element_type=jnp.float32) + enc_bias[None, :]
    listed = jnp.zeros((LATENTS,), jnp.float32).at[chat_ids].set(1.0)
    activity = jnp.where(listed[None, :] > 0.5, 0.0, jax.nn.relu(pre)).astype(jnp.bfloat16)
    spliced = (jnp.dot(activity, dec_weight, preferred_element_type=jnp.float32) + dec_bias[None, :]).astype(jnp.bfloat16)
    return (spliced, activity)
```

```python
import jax
import jax.numpy as jnp
from jax import lax
from jax.sharding import PartitionSpec as P

HEAD_DIM = 128


def gather_rows(x, count):
    copies = jnp.broadcast_to(x[None], (count,) + x.shape).reshape((count * x.shape[0],) + x.shape[1:])
    return lax.all_to_all(copies, "rows", split_axis=0, concat_axis=0, tiled=True)


def scatter_rows(x, count):
    got = lax.all_to_all(x, "rows", split_axis=0, concat_axis=0, tiled=True)
    return got.reshape((count, x.shape[0] // count) + x.shape[1:]).sum(axis=0)


def shards(
    queries,
    keys,
    values,
    lengths,
    resid,
    out_weight,
    chat_ids,
    enc_weight,
    enc_bias,
    dec_weight,
    dec_bias,
):
    count = lax.axis_size("rows")
    rows_here = queries.shape[0]
    cache_span = keys.shape[1]
    key_width = keys.shape[2]
    kv_count = key_width // HEAD_DIM
    group_size = queries.shape[1] // key_width
    query_heads = queries.reshape(rows_here, kv_count, group_size, HEAD_DIM)
    key_heads = keys.reshape(rows_here, cache_span, kv_count, HEAD_DIM)
    value_heads = values.reshape(rows_here, cache_span, kv_count, HEAD_DIM)
    scores = jnp.einsum(
        "rkgd,rskd->rkgs", query_heads, key_heads, preferred_element_type=jnp.float32
    )
    scores = scores / jnp.sqrt(jnp.float32(HEAD_DIM))
    visible = lax.broadcasted_iota(jnp.int32, (rows_here, cache_span), 1) < lengths[:, None]
    scores = jnp.where(visible[:, None, None, :], scores, -jnp.inf)
    highest = jnp.max(scores, axis=-1, keepdims=True)
    expo = jnp.exp(scores - highest)
    weights = (expo / jnp.sum(expo, axis=-1, keepdims=True)).astype(jnp.bfloat16)
    attended = jnp.einsum(
        "rkgs,rskd->rkgd", weights, value_heads, preferred_element_type=jnp.float32
    )
    attended = attended.astype(jnp.bfloat16).reshape(rows_here, kv_count * group_size * HEAD_DIM)
    features = lax.all_to_all(attended, "rows", split_axis=1, concat_axis=0, tiled=True)
    partial_value = jnp.dot(features, out_weight, preferred_element_type=jnp.float32)
    hidden_here = (scatter_rows(partial_value, count) + resid.astype(jnp.float32)).astype(jnp.bfloat16)
    hidden = gather_rows(hidden_here, count)
    lat_here = enc_weight.shape[1]
    latent_ids = lax.axis_index("rows") * lat_here + lax.broadcasted_iota(jnp.int32, (lat_here,), 0)
    listed = jnp.any(chat_ids[:, None] == latent_ids[None, :], axis=0)
    activity = jnp.where(
        listed[None, :],
        0.0,
        jax.nn.relu(
            jnp.dot(hidden, enc_weight, preferred_element_type=jnp.float32) + enc_bias[None, :]
        ),
    ).astype(jnp.bfloat16)
    rebuilt = scatter_rows(jnp.dot(activity, dec_weight, preferred_element_type=jnp.float32), count)
    spliced = (rebuilt + dec_bias[None, :]).astype(jnp.bfloat16)
    return (spliced, activity)


def solution(mesh):
    placed = (
        P(("groups", "rows"), None),
        P(("groups", "rows"), None, None),
        P(("groups", "rows"), None, None),
        P(("groups", "rows")),
        P(("groups", "rows"), None),
        P("rows", None),
        P(),
        P(None, "rows"),
        P("rows"),
        P("rows", None),
        P(),
    )
    return jax.shard_map(
        shards,
        mesh=mesh,
        in_specs=placed,
        out_specs=(P(("groups", "rows"), None), P("groups", "rows")),
        check_vma=False,
    )
```

```python
import math

import jax
import jax.numpy as jnp
from jax import lax
from jax.experimental import pallas as pl
from jax.experimental.pallas import tpu as pltpu
from jax.sharding import PartitionSpec as P

HEAD_DIM = 128


def attend_kernel(len_ref, q_ref, k_ref, v_ref, o_ref):
    span = k_ref.shape[1]
    kv_count = k_ref.shape[2] // HEAD_DIM
    group_size = q_ref.shape[1] // kv_count
    live = len_ref[pl.program_id(0)]
    queries = q_ref[0].astype(jnp.float32)
    scale = jnp.float32(math.sqrt(HEAD_DIM))
    outs = []
    for k in range(kv_count):
        qk = queries[k * group_size:(k + 1) * group_size].astype(jnp.bfloat16)
        kk = k_ref[0, :, k * HEAD_DIM:(k + 1) * HEAD_DIM]
        s = lax.dot_general(qk, kk, (((1,), (1,)), ((), ())), preferred_element_type=jnp.float32)
        s = s / scale
        pos = lax.broadcasted_iota(jnp.int32, s.shape, 1)
        s = jnp.where(pos < live, s, -jnp.inf)
        e = jnp.exp(s - jnp.max(s, axis=-1, keepdims=True))
        w = (e / jnp.sum(e, axis=-1, keepdims=True)).astype(jnp.bfloat16)
        vk = v_ref[0, :, k * HEAD_DIM:(k + 1) * HEAD_DIM]
        outs.append(jnp.dot(w, vk, preferred_element_type=jnp.float32))
    o_ref[0] = jnp.concatenate(outs, axis=0).astype(o_ref.dtype)


def attend(queries, keys, values, lengths):
    rows_here, span, key_width = keys.shape
    heads = queries.shape[1] // HEAD_DIM
    q3 = queries.reshape(rows_here, heads, HEAD_DIM)
    grid_spec = pltpu.PrefetchScalarGridSpec(
        num_scalar_prefetch=1,
        grid=(rows_here,),
        in_specs=[
            pl.BlockSpec((1, heads, HEAD_DIM), lambda i, n: (i, 0, 0)),
            pl.BlockSpec((1, span, key_width), lambda i, n: (i, 0, 0)),
            pl.BlockSpec((1, span, key_width), lambda i, n: (i, 0, 0)),
        ],
        out_specs=pl.BlockSpec((1, heads, HEAD_DIM), lambda i, n: (i, 0, 0)),
    )
    return pl.pallas_call(
        attend_kernel,
        grid_spec=grid_spec,
        out_shape=jax.ShapeDtypeStruct((rows_here, heads, HEAD_DIM), jnp.bfloat16),
    )(lengths, q3, keys, values)


def gather_rows(x, count):
    copies = jnp.tile(x, (count, 1))
    return lax.all_to_all(copies, "rows", split_axis=0, concat_axis=0, tiled=True)


def scatter_rows(x, count):
    got = lax.all_to_all(x, "rows", split_axis=0, concat_axis=0, tiled=True)
    return got.reshape((count, x.shape[0] // count) + x.shape[1:]).sum(axis=0)


def shards(
    queries,
    keys,
    values,
    lengths,
    resid,
    out_weight,
    chat_ids,
    enc_weight,
    enc_bias,
    dec_weight,
    dec_bias,
):
    count = lax.axis_size("rows")
    rows_here = queries.shape[0]
    attended = attend(queries, keys, values, lengths)
    attended = attended.reshape(rows_here, attended.shape[1] * HEAD_DIM)
    features = lax.all_to_all(attended, "rows", split_axis=1, concat_axis=0, tiled=True)
    partial_value = jnp.dot(features, out_weight, preferred_element_type=jnp.float32)
    hidden_here = (scatter_rows(partial_value, count) + resid.astype(jnp.float32)).astype(jnp.bfloat16)
    hidden = gather_rows(hidden_here, count)
    lat_here = enc_weight.shape[1]
    latent_ids = lax.axis_index("rows") * lat_here + lax.broadcasted_iota(jnp.int32, (lat_here,), 0)
    listed = jnp.any(chat_ids[:, None] == latent_ids[None, :], axis=0)
    activity = jnp.where(
        listed[None, :],
        0.0,
        jax.nn.relu(
            jnp.dot(hidden, enc_weight, preferred_element_type=jnp.float32) + enc_bias[None, :]
        ),
    ).astype(jnp.bfloat16)
    rebuilt = scatter_rows(jnp.dot(activity, dec_weight, preferred_element_type=jnp.float32), count)
    spliced = (rebuilt + dec_bias[None, :]).astype(jnp.bfloat16)
    return (spliced, activity)


def solution(mesh):
    placed = (
        P(("groups", "rows"), None),
        P(("groups", "rows"), None, None),
        P(("groups", "rows"), None, None),
        P(("groups", "rows")),
        P(("groups", "rows"), None),
        P("rows", None),
        P(),
        P(None, "rows"),
        P("rows"),
        P("rows", None),
        P(),
    )
    return jax.shard_map(
        shards,
        mesh=mesh,
        in_specs=placed,
        out_specs=(P(("groups", "rows"), None), P("groups", "rows")),
        check_vma=False,
    )
```

```python
import jax
import jax.numpy as jnp
from jax import lax
from jax.sharding import PartitionSpec as P

HEAD_DIM = 128


def gather_rows(x, count):
    halves = x.reshape(2 * x.shape[0], x.shape[1] // 2)
    copies = jnp.broadcast_to(halves[None], (count,) + halves.shape).reshape((count * halves.shape[0], halves.shape[1]))
    got = lax.all_to_all(copies, "rows", split_axis=0, concat_axis=0, tiled=True)
    return got.reshape(count * x.shape[0], x.shape[1])


def scatter_rows(x, count):
    got = lax.all_to_all(x, "rows", split_axis=0, concat_axis=0, tiled=True)
    return got.reshape((count, x.shape[0] // count) + x.shape[1:]).sum(axis=0)


def shards(
    queries,
    keys,
    values,
    lengths,
    resid,
    out_weight,
    chat_ids,
    enc_weight,
    enc_bias,
    dec_weight,
    dec_bias,
):
    count = lax.axis_size("rows")
    rows_here = queries.shape[0]
    cache_span = keys.shape[1]
    key_width = keys.shape[2]
    kv_count = key_width // HEAD_DIM
    group_size = queries.shape[1] // key_width
    query_heads = queries.reshape(rows_here, kv_count, group_size, HEAD_DIM)
    key_heads = keys.reshape(rows_here, cache_span, kv_count, HEAD_DIM)
    value_heads = values.reshape(rows_here, cache_span, kv_count, HEAD_DIM)
    scores = jnp.einsum(
        "rkgd,rskd->rkgs", query_heads, key_heads, preferred_element_type=jnp.float32
    )
    scores = scores / jnp.sqrt(jnp.float32(HEAD_DIM))
    visible = lax.broadcasted_iota(jnp.int32, (rows_here, cache_span), 1) < lengths[:, None]
    scores = jnp.where(visible[:, None, None, :], scores, -jnp.inf)
    highest = jnp.max(scores, axis=-1, keepdims=True)
    expo = jnp.exp(scores - highest)
    weights = (expo / jnp.sum(expo, axis=-1, keepdims=True)).astype(jnp.bfloat16)
    attended = jnp.einsum(
        "rkgs,rskd->rkgd", weights, value_heads, preferred_element_type=jnp.float32
    )
    attended = attended.astype(jnp.bfloat16).reshape(rows_here, kv_count * group_size * HEAD_DIM)
    features = lax.all_to_all(attended, "rows", split_axis=1, concat_axis=0, tiled=True)
    partial_value = jnp.dot(features, out_weight, preferred_element_type=jnp.float32)
    hidden_here = (scatter_rows(partial_value, count) + resid.astype(jnp.float32)).astype(jnp.bfloat16)
    hidden = gather_rows(hidden_here, count)
    lat_here = enc_weight.shape[1]
    latent_ids = lax.axis_index("rows") * lat_here + lax.broadcasted_iota(jnp.int32, (lat_here,), 0)
    listed = jnp.any(chat_ids[:, None] == latent_ids[None, :], axis=0)
    activity = jnp.where(
        listed[None, :],
        0.0,
        jax.nn.relu(
            jnp.dot(hidden, enc_weight, preferred_element_type=jnp.float32) + enc_bias[None, :]
        ),
    ).astype(jnp.bfloat16)
    rebuilt = scatter_rows(jnp.dot(activity, dec_weight, preferred_element_type=jnp.float32), count)
    spliced = (rebuilt + dec_bias[None, :]).astype(jnp.bfloat16)
    return (spliced, activity)


def solution(mesh):
    placed = (
        P(("groups", "rows"), None),
        P(("groups", "rows"), None, None),
        P(("groups", "rows"), None, None),
        P(("groups", "rows")),
        P(("groups", "rows"), None),
        P("rows", None),
        P(),
        P(None, "rows"),
        P("rows"),
        P("rows", None),
        P(),
    )
    return jax.shard_map(
        shards,
        mesh=mesh,
        in_specs=placed,
        out_specs=(P(("groups", "rows"), None), P("groups", "rows")),
        check_vma=False,
    )
```

```python
import jax
import jax.numpy as jnp
from jax import lax
from jax.sharding import PartitionSpec as P

HEAD_DIM = 128


def gather_rows(x, count):
    halves = x.reshape(2 * x.shape[0], x.shape[1] // 2)
    copies = jnp.broadcast_to(halves[None], (count,) + halves.shape).reshape((count * halves.shape[0], halves.shape[1]))
    got = lax.all_to_all(copies, "rows", split_axis=0, concat_axis=0, tiled=True)
    return got.reshape(count * x.shape[0], x.shape[1])


def scatter_rows(x, count):
    got = lax.all_to_all(x, "rows", split_axis=0, concat_axis=0, tiled=True)
    return got.reshape((count, x.shape[0] // count) + x.shape[1:]).sum(axis=0)


def shards(
    queries,
    keys,
    values,
    lengths,
    resid,
    out_weight,
    chat_ids,
    enc_weight,
    enc_bias,
    dec_weight,
    dec_bias,
):
    count = lax.axis_size("rows")
    rows_here = queries.shape[0]
    key_width = keys.shape[2]
    kv_count = key_width // HEAD_DIM
    heads = queries.shape[1] // HEAD_DIM
    group_size = heads // kv_count
    head_of = lax.broadcasted_iota(jnp.int32, (heads, kv_count), 0) // group_size
    block_of = lax.broadcasted_iota(jnp.int32, (heads, kv_count), 1)
    onehot = (head_of == block_of).astype(jnp.bfloat16)
    query_heads = queries.reshape(rows_here, heads, 1, HEAD_DIM)
    spread = (query_heads * onehot[None, :, :, None]).reshape(rows_here, heads, key_width)
    scores = jnp.einsum("rhc,rsc->rhs", spread, keys, preferred_element_type=jnp.float32)
    scores = scores / jnp.sqrt(jnp.float32(HEAD_DIM))
    cache_span = keys.shape[1]
    visible = lax.broadcasted_iota(jnp.int32, (rows_here, cache_span), 1) < lengths[:, None]
    scores = jnp.where(visible[:, None, :], scores, -jnp.inf)
    highest = jnp.max(scores, axis=-1, keepdims=True)
    expo = jnp.exp(scores - highest)
    weights = (expo / jnp.sum(expo, axis=-1, keepdims=True)).astype(jnp.bfloat16)
    mixed = jnp.einsum("rhs,rsc->rhc", weights, values, preferred_element_type=jnp.float32)
    mixed = mixed.reshape(rows_here, heads, kv_count, HEAD_DIM) * onehot.astype(jnp.float32)[None, :, :, None]
    attended = mixed.sum(axis=2).astype(jnp.bfloat16).reshape(rows_here, heads * HEAD_DIM)
    features = lax.all_to_all(attended, "rows", split_axis=1, concat_axis=0, tiled=True)
    partial_value = jnp.dot(features, out_weight, preferred_element_type=jnp.float32)
    hidden_here = (scatter_rows(partial_value, count) + resid.astype(jnp.float32)).astype(jnp.bfloat16)
    hidden = gather_rows(hidden_here, count)
    lat_here = enc_weight.shape[1]
    latent_ids = lax.axis_index("rows") * lat_here + lax.broadcasted_iota(jnp.int32, (lat_here,), 0)
    listed = jnp.any(chat_ids[:, None] == latent_ids[None, :], axis=0)
    activity = jnp.where(
        listed[None, :],
        0.0,
        jax.nn.relu(
            jnp.dot(hidden, enc_weight, preferred_element_type=jnp.float32) + enc_bias[None, :]
        ),
    ).astype(jnp.bfloat16)
    rebuilt = scatter_rows(jnp.dot(activity, dec_weight, preferred_element_type=jnp.float32), count)
    spliced = (rebuilt + dec_bias[None, :]).astype(jnp.bfloat16)
    return (spliced, activity)


def solution(mesh):
    placed = (
        P(("groups", "rows"), None),
        P(("groups", "rows"), None, None),
        P(("groups", "rows"), None, None),
        P(("groups", "rows")),
        P(("groups", "rows"), None),
        P("rows", None),
        P(),
        P(None, "rows"),
        P("rows"),
        P("rows", None),
        P(),
    )
    return jax.shard_map(
        shards,
        mesh=mesh,
        in_specs=placed,
        out_specs=(P(("groups", "rows"), None), P("groups", "rows")),
        check_vma=False,
    )
```

```python
import jax
import jax.numpy as jnp
from jax import lax
from jax.sharding import PartitionSpec as P

HEAD_DIM = 128


def gather_rows(x, count):
    halves = x.reshape(2 * x.shape[0], x.shape[1] // 2)
    copies = jnp.broadcast_to(halves[None], (count,) + halves.shape).reshape((count * halves.shape[0], halves.shape[1]))
    got = lax.all_to_all(copies, "rows", split_axis=0, concat_axis=0, tiled=True)
    return got.reshape(count * x.shape[0], x.shape[1])


def scatter_rows(x, count):
    got = lax.all_to_all(x, "rows", split_axis=0, concat_axis=0, tiled=True)
    return got.reshape((count, x.shape[0] // count) + x.shape[1:]).sum(axis=0)


def shards(
    queries,
    keys,
    values,
    lengths,
    resid,
    out_weight,
    chat_ids,
    enc_weight,
    enc_bias,
    dec_weight,
    dec_bias,
):
    count = lax.axis_size("rows")
    rows_here = queries.shape[0]
    key_width = keys.shape[2]
    kv_count = key_width // HEAD_DIM
    heads = queries.shape[1] // HEAD_DIM
    group_size = heads // kv_count
    head_of = lax.broadcasted_iota(jnp.int32, (heads, kv_count), 0) // group_size
    block_of = lax.broadcasted_iota(jnp.int32, (heads, kv_count), 1)
    onehot = (head_of == block_of).astype(jnp.bfloat16)
    query_heads = queries.reshape(rows_here, heads, 1, HEAD_DIM)
    spread = (query_heads * onehot[None, :, :, None]).reshape(rows_here, heads, key_width)
    scores = jnp.einsum("rhc,rsc->rhs", spread, keys, preferred_element_type=jnp.float32)
    scores = scores / jnp.sqrt(jnp.float32(HEAD_DIM))
    cache_span = keys.shape[1]
    visible = lax.broadcasted_iota(jnp.int32, (rows_here, cache_span), 1) < lengths[:, None]
    scores = jnp.where(visible[:, None, :], scores, -jnp.inf)
    highest = jnp.max(scores, axis=-1, keepdims=True)
    expo = jnp.exp(scores - highest)
    weights = (expo / jnp.sum(expo, axis=-1, keepdims=True)).astype(jnp.bfloat16)
    mixed = jnp.einsum("rhs,rsc->rhc", weights, values, preferred_element_type=jnp.float32)
    mixed = lax.optimization_barrier(mixed).reshape(rows_here, heads, kv_count, HEAD_DIM) * onehot.astype(jnp.float32)[None, :, :, None]
    attended = mixed.sum(axis=2).astype(jnp.bfloat16).reshape(rows_here, heads * HEAD_DIM)
    features = lax.all_to_all(attended, "rows", split_axis=1, concat_axis=0, tiled=True)
    partial_value = jnp.dot(features, out_weight, preferred_element_type=jnp.float32)
    hidden_here = (scatter_rows(partial_value, count) + resid.astype(jnp.float32)).astype(jnp.bfloat16)
    hidden = gather_rows(hidden_here, count)
    lat_here = enc_weight.shape[1]
    latent_ids = lax.axis_index("rows") * lat_here + lax.broadcasted_iota(jnp.int32, (lat_here,), 0)
    listed = jnp.any(chat_ids[:, None] == latent_ids[None, :], axis=0)
    activity = jnp.where(
        listed[None, :],
        0.0,
        jax.nn.relu(
            jnp.dot(hidden, enc_weight, preferred_element_type=jnp.float32) + enc_bias[None, :]
        ),
    ).astype(jnp.bfloat16)
    rebuilt = scatter_rows(jnp.dot(activity, dec_weight, preferred_element_type=jnp.float32), count)
    spliced = (rebuilt + dec_bias[None, :]).astype(jnp.bfloat16)
    return (spliced, activity)


def solution(mesh):
    placed = (
        P(("groups", "rows"), None),
        P(("groups", "rows"), None, None),
        P(("groups", "rows"), None, None),
        P(("groups", "rows")),
        P(("groups", "rows"), None),
        P("rows", None),
        P(),
        P(None, "rows"),
        P("rows"),
        P("rows", None),
        P(),
    )
    return jax.shard_map(
        shards,
        mesh=mesh,
        in_specs=placed,
        out_specs=(P(("groups", "rows"), None), P("groups", "rows")),
        check_vma=False,
    )
```

```python
import jax
import jax.numpy as jnp
from jax import lax
from jax.sharding import Mesh, PartitionSpec as P

HEAD_DIM = 128


ROWS = ("chip", "core")


def pick(pair, first):
    return jnp.where(lax.axis_index("core") == first, pair[0], pair[1])


def gather_rows(x, chips):
    halves = x.reshape(2 * x.shape[0], x.shape[1] // 2)
    copies = jnp.broadcast_to(halves[None], (chips,) + halves.shape).reshape((chips * halves.shape[0], halves.shape[1]))
    mine = lax.all_to_all(copies, "chip", split_axis=0, concat_axis=0, tiled=True)
    mine = mine.reshape(chips, x.shape[0], x.shape[1])
    mate = lax.ppermute(mine, "core", [(0, 1), (1, 0)])
    first = pick((mine, mate), 0)
    second = pick((mate, mine), 0)
    return jnp.stack([first, second], axis=1).reshape(chips * 2 * x.shape[0], x.shape[1])


def scatter_rows(x, chips):
    per = x.shape[0] // (2 * chips)
    split = x.reshape(chips, 2, per, x.shape[1])
    keep = pick((split[:, 0], split[:, 1]), 0)
    give = pick((split[:, 1], split[:, 0]), 0)
    summed = keep + lax.ppermute(give, "core", [(0, 1), (1, 0)])
    got = lax.all_to_all(summed.reshape(chips * per, x.shape[1]), "chip", split_axis=0, concat_axis=0, tiled=True)
    return got.reshape(chips, per, x.shape[1]).sum(axis=0)


def shards(
    queries,
    keys,
    values,
    lengths,
    resid,
    out_weight,
    chat_ids,
    enc_weight,
    enc_bias,
    dec_weight,
    dec_bias,
):
    chips = lax.axis_size("chip")
    rows_here = queries.shape[0]
    key_width = keys.shape[2]
    kv_count = key_width // HEAD_DIM
    heads = queries.shape[1] // HEAD_DIM
    group_size = heads // kv_count
    head_of = lax.broadcasted_iota(jnp.int32, (heads, kv_count), 0) // group_size
    block_of = lax.broadcasted_iota(jnp.int32, (heads, kv_count), 1)
    onehot = (head_of == block_of).astype(jnp.bfloat16)
    query_heads = queries.reshape(rows_here, heads, 1, HEAD_DIM)
    spread = (query_heads * onehot[None, :, :, None]).reshape(rows_here, heads, key_width)
    scores = jnp.einsum("rhc,rsc->rhs", spread, keys, preferred_element_type=jnp.float32)
    scores = scores / jnp.sqrt(jnp.float32(HEAD_DIM))
    cache_span = keys.shape[1]
    visible = lax.broadcasted_iota(jnp.int32, (rows_here, cache_span), 1) < lengths[:, None]
    scores = jnp.where(visible[:, None, :], scores, -jnp.inf)
    highest = jnp.max(scores, axis=-1, keepdims=True)
    expo = jnp.exp(scores - highest)
    weights = (expo / jnp.sum(expo, axis=-1, keepdims=True)).astype(jnp.bfloat16)
    mixed = jnp.einsum("rhs,rsc->rhc", weights, values, preferred_element_type=jnp.float32)
    mixed = lax.optimization_barrier(mixed).reshape(rows_here, heads, kv_count, HEAD_DIM) * onehot.astype(jnp.float32)[None, :, :, None]
    attended = mixed.sum(axis=2).astype(jnp.bfloat16).reshape(rows_here, heads * HEAD_DIM)
    features = lax.all_to_all(attended, ROWS, split_axis=1, concat_axis=0, tiled=True)
    partial_value = jnp.dot(features, out_weight, preferred_element_type=jnp.float32)
    hidden_here = (scatter_rows(partial_value, chips) + resid.astype(jnp.float32)).astype(jnp.bfloat16)
    hidden = gather_rows(hidden_here, chips)
    lat_here = enc_weight.shape[1]
    latent_ids = lax.axis_index(ROWS) * lat_here + lax.broadcasted_iota(jnp.int32, (lat_here,), 0)
    listed = jnp.any(chat_ids[:, None] == latent_ids[None, :], axis=0)
    activity = jnp.where(
        listed[None, :],
        0.0,
        jax.nn.relu(
            jnp.dot(hidden, enc_weight, preferred_element_type=jnp.float32) + enc_bias[None, :]
        ),
    ).astype(jnp.bfloat16)
    rebuilt = scatter_rows(jnp.dot(activity, dec_weight, preferred_element_type=jnp.float32), chips)
    spliced = (rebuilt + dec_bias[None, :]).astype(jnp.bfloat16)
    return (spliced, activity)


def solution(mesh):
    groups, count = mesh.devices.shape
    paired = Mesh(mesh.devices.reshape(groups, count // 2, 2), ("groups",) + ROWS)
    lead = ("groups",) + ROWS
    placed = (
        P(lead, None),
        P(lead, None, None),
        P(lead, None, None),
        P(lead),
        P(lead, None),
        P(ROWS, None),
        P(),
        P(None, ROWS),
        P(ROWS),
        P(ROWS, None),
        P(),
    )
    return jax.shard_map(
        shards,
        mesh=paired,
        in_specs=placed,
        out_specs=(P(lead, None), P("groups", ROWS)),
        check_vma=False,
    )
```

```python
import jax
import jax.numpy as jnp
from jax import lax
from jax.sharding import Mesh, PartitionSpec as P

HEAD_DIM = 128


ROWS = ("chip", "core")


def pick(pair, first):
    return jnp.where(lax.axis_index("core") == first, pair[0], pair[1])


def gather_rows(x, chips):
    halves = x.reshape(2 * x.shape[0], x.shape[1] // 2)
    copies = jnp.broadcast_to(halves[None], (chips,) + halves.shape).reshape((chips * halves.shape[0], halves.shape[1]))
    mine = lax.all_to_all(copies, "chip", split_axis=0, concat_axis=0, tiled=True)
    mine = mine.reshape(chips, x.shape[0], x.shape[1])
    mate = lax.ppermute(mine, "core", [(0, 1), (1, 0)])
    first = pick((mine, mate), 0)
    second = pick((mate, mine), 0)
    return jnp.stack([first, second], axis=1).reshape(chips * 2 * x.shape[0], x.shape[1])


def scatter_rows(x, chips):
    per = x.shape[0] // (2 * chips)
    split = x.reshape(chips, 2, per, x.shape[1])
    keep = pick((split[:, 0], split[:, 1]), 0)
    give = pick((split[:, 1], split[:, 0]), 0)
    summed = keep + lax.ppermute(give, "core", [(0, 1), (1, 0)])
    got = lax.all_to_all(summed.reshape(chips * per, x.shape[1]), "chip", split_axis=0, concat_axis=0, tiled=True)
    return got.reshape(chips, per, x.shape[1]).sum(axis=0)


def shards(
    queries,
    keys,
    values,
    lengths,
    resid,
    out_weight,
    chat_ids,
    enc_weight,
    enc_bias,
    dec_weight,
    dec_bias,
):
    chips = lax.axis_size("chip")
    rows_here = queries.shape[0]
    key_width = keys.shape[2]
    kv_count = key_width // HEAD_DIM
    heads = queries.shape[1] // HEAD_DIM
    group_size = heads // kv_count
    head_of = lax.broadcasted_iota(jnp.int32, (heads, kv_count), 0) // group_size
    block_of = lax.broadcasted_iota(jnp.int32, (heads, kv_count), 1)
    onehot = (head_of == block_of).astype(jnp.bfloat16)
    query_heads = queries.reshape(rows_here, heads, 1, HEAD_DIM)
    spread = (query_heads * onehot[None, :, :, None]).reshape(rows_here, heads, key_width)
    scores = jnp.einsum("rhc,rsc->rhs", spread, keys, preferred_element_type=jnp.float32)
    scores = scores / jnp.sqrt(jnp.float32(HEAD_DIM))
    cache_span = keys.shape[1]
    visible = lax.broadcasted_iota(jnp.int32, (rows_here, cache_span), 1) < lengths[:, None]
    scores = jnp.where(visible[:, None, :], scores, -jnp.inf)
    highest = jnp.max(scores, axis=-1, keepdims=True)
    expo = jnp.exp(scores - highest)
    weights = (expo / jnp.sum(expo, axis=-1, keepdims=True)).astype(jnp.bfloat16)
    mixed = jnp.einsum("rhs,rsc->rhc", weights, values, preferred_element_type=jnp.float32)
    mixed = lax.optimization_barrier(mixed).reshape(rows_here, heads, kv_count, HEAD_DIM) * onehot.astype(jnp.float32)[None, :, :, None]
    attended = mixed.sum(axis=2).astype(jnp.bfloat16)
    count = 2 * chips
    if heads % count == 0:
        blocks = attended.reshape(rows_here * count, heads // count, HEAD_DIM)
        got = lax.all_to_all(blocks, ROWS, split_axis=0, concat_axis=0, tiled=True)
        features = got.reshape(count * rows_here, (heads // count) * HEAD_DIM)
    else:
        attended = attended.reshape(rows_here, heads * HEAD_DIM)
        features = lax.all_to_all(attended, ROWS, split_axis=1, concat_axis=0, tiled=True)
    partial_value = jnp.dot(features, out_weight, preferred_element_type=jnp.float32)
    hidden_here = (scatter_rows(partial_value, chips) + resid.astype(jnp.float32)).astype(jnp.bfloat16)
    hidden = gather_rows(hidden_here, chips)
    lat_here = enc_weight.shape[1]
    latent_ids = lax.axis_index(ROWS) * lat_here + lax.broadcasted_iota(jnp.int32, (lat_here,), 0)
    listed = jnp.any(chat_ids[:, None] == latent_ids[None, :], axis=0)
    activity = jnp.where(
        listed[None, :],
        0.0,
        jax.nn.relu(
            jnp.dot(hidden, enc_weight, preferred_element_type=jnp.float32) + enc_bias[None, :]
        ),
    ).astype(jnp.bfloat16)
    rebuilt = scatter_rows(jnp.dot(activity, dec_weight, preferred_element_type=jnp.float32), chips)
    spliced = (rebuilt + dec_bias[None, :]).astype(jnp.bfloat16)
    return (spliced, activity)


def solution(mesh):
    groups, count = mesh.devices.shape
    paired = Mesh(mesh.devices.reshape(groups, count // 2, 2), ("groups",) + ROWS)
    lead = ("groups",) + ROWS
    placed = (
        P(lead, None),
        P(lead, None, None),
        P(lead, None, None),
        P(lead),
        P(lead, None),
        P(ROWS, None),
        P(),
        P(None, ROWS),
        P(ROWS),
        P(ROWS, None),
        P(),
    )
    return jax.shard_map(
        shards,
        mesh=paired,
        in_specs=placed,
        out_specs=(P(lead, None), P("groups", ROWS)),
        check_vma=False,
    )
```

```python
import jax
import jax.numpy as jnp
from jax import lax
from jax.sharding import Mesh, PartitionSpec as P

HEAD_DIM = 128


ROWS = ("chip", "core")


def pick(pair, first):
    return jnp.where(lax.axis_index("core") == first, pair[0], pair[1])


def gather_rows(x, chips):
    halves = x.reshape(2 * x.shape[0], x.shape[1] // 2)
    copies = jnp.broadcast_to(halves[None], (chips,) + halves.shape).reshape((chips * halves.shape[0], halves.shape[1]))
    mine = lax.all_to_all(copies, "chip", split_axis=0, concat_axis=0, tiled=True)
    mine = mine.reshape(chips, x.shape[0], x.shape[1])
    mate = lax.ppermute(mine, "core", [(0, 1), (1, 0)])
    first = pick((mine, mate), 0)
    second = pick((mate, mine), 0)
    return jnp.stack([first, second], axis=1).reshape(chips * 2 * x.shape[0], x.shape[1])


def scatter_rows(x, chips, narrow=False):
    per = x.shape[0] // (2 * chips)
    split = x.reshape(chips, 2, per, x.shape[1])
    keep = pick((split[:, 0], split[:, 1]), 0)
    give = pick((split[:, 1], split[:, 0]), 0)
    summed = keep + lax.ppermute(give, "core", [(0, 1), (1, 0)])
    if narrow:
        sent = summed.astype(jnp.bfloat16).reshape(chips * per * 2, x.shape[1] // 2)
        got = lax.all_to_all(sent, "chip", split_axis=0, concat_axis=0, tiled=True)
        return got.astype(jnp.float32).reshape(chips, per, x.shape[1]).sum(axis=0)
    got = lax.all_to_all(summed.reshape(chips * per, x.shape[1]), "chip", split_axis=0, concat_axis=0, tiled=True)
    return got.reshape(chips, per, x.shape[1]).sum(axis=0)


def shards(
    queries,
    keys,
    values,
    lengths,
    resid,
    out_weight,
    chat_ids,
    enc_weight,
    enc_bias,
    dec_weight,
    dec_bias,
):
    chips = lax.axis_size("chip")
    rows_here = queries.shape[0]
    key_width = keys.shape[2]
    kv_count = key_width // HEAD_DIM
    heads = queries.shape[1] // HEAD_DIM
    group_size = heads // kv_count
    head_of = lax.broadcasted_iota(jnp.int32, (heads, kv_count), 0) // group_size
    block_of = lax.broadcasted_iota(jnp.int32, (heads, kv_count), 1)
    onehot = (head_of == block_of).astype(jnp.bfloat16)
    query_heads = queries.reshape(rows_here, heads, 1, HEAD_DIM)
    spread = (query_heads * onehot[None, :, :, None]).reshape(rows_here, heads, key_width)
    scores = jnp.einsum("rhc,rsc->rhs", spread, keys, preferred_element_type=jnp.float32)
    scores = scores / jnp.sqrt(jnp.float32(HEAD_DIM))
    cache_span = keys.shape[1]
    visible = lax.broadcasted_iota(jnp.int32, (rows_here, cache_span), 1) < lengths[:, None]
    scores = jnp.where(visible[:, None, :], scores, -jnp.inf)
    highest = jnp.max(scores, axis=-1, keepdims=True)
    expo = jnp.exp(scores - highest)
    weights = (expo / jnp.sum(expo, axis=-1, keepdims=True)).astype(jnp.bfloat16)
    mixed = jnp.einsum("rhs,rsc->rhc", weights, values, preferred_element_type=jnp.float32)
    mixed = lax.optimization_barrier(mixed).reshape(rows_here, heads, kv_count, HEAD_DIM) * onehot.astype(jnp.float32)[None, :, :, None]
    attended = mixed.sum(axis=2).astype(jnp.bfloat16)
    count = 2 * chips
    if heads % count == 0:
        blocks = attended.reshape(rows_here * count, heads // count, HEAD_DIM)
        got = lax.all_to_all(blocks, ROWS, split_axis=0, concat_axis=0, tiled=True)
        features = got.reshape(count * rows_here, (heads // count) * HEAD_DIM)
    else:
        attended = attended.reshape(rows_here, heads * HEAD_DIM)
        features = lax.all_to_all(attended, ROWS, split_axis=1, concat_axis=0, tiled=True)
    partial_value = jnp.dot(features, out_weight, preferred_element_type=jnp.float32)
    hidden_here = (scatter_rows(partial_value, chips) + resid.astype(jnp.float32)).astype(jnp.bfloat16)
    hidden = gather_rows(hidden_here, chips)
    lat_here = enc_weight.shape[1]
    latent_ids = lax.axis_index(ROWS) * lat_here + lax.broadcasted_iota(jnp.int32, (lat_here,), 0)
    listed = jnp.any(chat_ids[:, None] == latent_ids[None, :], axis=0)
    activity = jnp.where(
        listed[None, :],
        0.0,
        jax.nn.relu(
            jnp.dot(hidden, enc_weight, preferred_element_type=jnp.float32) + enc_bias[None, :]
        ),
    ).astype(jnp.bfloat16)
    rebuilt = scatter_rows(jnp.dot(activity, dec_weight, preferred_element_type=jnp.float32), chips, narrow=True)
    spliced = (rebuilt + dec_bias[None, :]).astype(jnp.bfloat16)
    return (spliced, activity)


def solution(mesh):
    groups, count = mesh.devices.shape
    paired = Mesh(mesh.devices.reshape(groups, count // 2, 2), ("groups",) + ROWS)
    lead = ("groups",) + ROWS
    placed = (
        P(lead, None),
        P(lead, None, None),
        P(lead, None, None),
        P(lead),
        P(lead, None),
        P(ROWS, None),
        P(),
        P(None, ROWS),
        P(ROWS),
        P(ROWS, None),
        P(),
    )
    return jax.shard_map(
        shards,
        mesh=paired,
        in_specs=placed,
        out_specs=(P(lead, None), P("groups", ROWS)),
        check_vma=False,
    )
```

```python
import jax
import jax.numpy as jnp
from jax import lax
from jax.sharding import Mesh, PartitionSpec as P

HEAD_DIM = 128


ROWS = ("chip", "core")


def pick(pair, first):
    return jnp.where(lax.axis_index("core") == first, pair[0], pair[1])


def gather_rows(x, chips):
    halves = x.reshape(2 * x.shape[0], x.shape[1] // 2)
    copies = jnp.broadcast_to(halves[None], (chips,) + halves.shape).reshape((chips * halves.shape[0], halves.shape[1]))
    mine = lax.all_to_all(copies, "chip", split_axis=0, concat_axis=0, tiled=True)
    mine = mine.reshape(chips, x.shape[0], x.shape[1])
    mate = lax.ppermute(mine, "core", [(0, 1), (1, 0)])
    first = pick((mine, mate), 0)
    second = pick((mate, mine), 0)
    return jnp.stack([first, second], axis=1).reshape(chips * 2 * x.shape[0], x.shape[1])


def scatter_rows(x, chips, narrow=False):
    per = x.shape[0] // (2 * chips)
    split = x.reshape(chips, 2, per, x.shape[1])
    keep = pick((split[:, 0], split[:, 1]), 0)
    give = pick((split[:, 1], split[:, 0]), 0)
    summed = keep + lax.ppermute(give, "core", [(0, 1), (1, 0)])
    if narrow:
        sent = summed.astype(jnp.bfloat16).reshape(chips * per * 2, x.shape[1] // 2)
        got = lax.all_to_all(sent, "chip", split_axis=0, concat_axis=0, tiled=True)
        return got.astype(jnp.float32).reshape(chips, per, x.shape[1]).sum(axis=0)
    got = lax.all_to_all(summed.reshape(chips * per, x.shape[1]), "chip", split_axis=0, concat_axis=0, tiled=True)
    return got.reshape(chips, per, x.shape[1]).sum(axis=0)


def shards(
    queries,
    keys,
    values,
    lengths,
    resid,
    out_weight,
    chat_ids,
    enc_weight,
    enc_bias,
    dec_weight,
    dec_bias,
):
    chips = lax.axis_size("chip")
    rows_here = queries.shape[0]
    key_width = keys.shape[2]
    kv_count = key_width // HEAD_DIM
    heads = queries.shape[1] // HEAD_DIM
    group_size = heads // kv_count
    head_of = lax.broadcasted_iota(jnp.int32, (heads, kv_count), 0) // group_size
    block_of = lax.broadcasted_iota(jnp.int32, (heads, kv_count), 1)
    onehot = (head_of == block_of).astype(jnp.bfloat16)
    query_heads = queries.reshape(rows_here, heads, 1, HEAD_DIM)
    spread = (query_heads * onehot[None, :, :, None]).reshape(rows_here, heads, key_width)
    scores = jnp.einsum("rhc,rsc->rhs", spread, keys, preferred_element_type=jnp.float32)
    scores = scores / jnp.sqrt(jnp.float32(HEAD_DIM))
    cache_span = keys.shape[1]
    visible = lax.broadcasted_iota(jnp.int32, (rows_here, cache_span), 1) < lengths[:, None]
    scores = jnp.where(visible[:, None, :], scores, -jnp.inf)
    highest = jnp.max(scores, axis=-1, keepdims=True)
    expo = jnp.exp(scores - highest)
    weights = (expo / jnp.sum(expo, axis=-1, keepdims=True)).astype(jnp.bfloat16)
    mixed = jnp.einsum("rhs,rsc->rhc", weights, values, preferred_element_type=jnp.float32)
    mixed = lax.optimization_barrier(mixed).reshape(rows_here, heads, kv_count, HEAD_DIM) * onehot.astype(jnp.float32)[None, :, :, None]
    attended = mixed.sum(axis=2).astype(jnp.bfloat16)
    count = 2 * chips
    if heads % count == 0:
        blocks = attended.reshape(rows_here * count, heads // count, HEAD_DIM)
        got = lax.all_to_all(blocks, ROWS, split_axis=0, concat_axis=0, tiled=True)
        features = got.reshape(count * rows_here, (heads // count) * HEAD_DIM)
    else:
        attended = attended.reshape(rows_here, heads * HEAD_DIM)
        features = lax.all_to_all(attended, ROWS, split_axis=1, concat_axis=0, tiled=True)
    partial_value = jnp.dot(features, out_weight, preferred_element_type=jnp.float32)
    hidden_here = (scatter_rows(partial_value, chips, narrow=True) + resid.astype(jnp.float32)).astype(jnp.bfloat16)
    hidden = gather_rows(hidden_here, chips)
    lat_here = enc_weight.shape[1]
    latent_ids = lax.axis_index(ROWS) * lat_here + lax.broadcasted_iota(jnp.int32, (lat_here,), 0)
    listed = jnp.any(chat_ids[:, None] == latent_ids[None, :], axis=0)
    activity = jnp.where(
        listed[None, :],
        0.0,
        jax.nn.relu(
            jnp.dot(hidden, enc_weight, preferred_element_type=jnp.float32) + enc_bias[None, :]
        ),
    ).astype(jnp.bfloat16)
    rebuilt = scatter_rows(jnp.dot(activity, dec_weight, preferred_element_type=jnp.float32), chips, narrow=True)
    spliced = (rebuilt + dec_bias[None, :]).astype(jnp.bfloat16)
    return (spliced, activity)


def solution(mesh):
    groups, count = mesh.devices.shape
    paired = Mesh(mesh.devices.reshape(groups, count // 2, 2), ("groups",) + ROWS)
    lead = ("groups",) + ROWS
    placed = (
        P(lead, None),
        P(lead, None, None),
        P(lead, None, None),
        P(lead),
        P(lead, None),
        P(ROWS, None),
        P(),
        P(None, ROWS),
        P(ROWS),
        P(ROWS, None),
        P(),
    )
    return jax.shard_map(
        shards,
        mesh=paired,
        in_specs=placed,
        out_specs=(P(lead, None), P("groups", ROWS)),
        check_vma=False,
    )
```

```python
import jax
from jax.experimental import pallas as pl
from jax.experimental.pallas import tpu as pltpu
import jax.numpy as jnp
from jax import lax
from jax.sharding import Mesh, PartitionSpec as P

HEAD_DIM = 128


def attend_kernel(len_ref, q_ref, k_ref, v_ref, o_ref):
    live = len_ref[pl.program_id(0)]
    s = lax.dot_general(q_ref[...], k_ref[0], (((1,), (1,)), ((), ())), preferred_element_type=jnp.float32)
    s = s / jnp.sqrt(jnp.float32(HEAD_DIM))
    pos = lax.broadcasted_iota(jnp.int32, s.shape, 1)
    s = jnp.where(pos < live, s, -jnp.inf)
    e = jnp.exp(s - jnp.max(s, axis=-1, keepdims=True))
    w = (e / jnp.sum(e, axis=-1, keepdims=True)).astype(jnp.bfloat16)
    o_ref[...] = jnp.dot(w, v_ref[0], preferred_element_type=jnp.float32).astype(o_ref.dtype)


def attend(queries, keys, values, lengths):
    rows_here, span, key_width = keys.shape
    kv_count = key_width // HEAD_DIM
    heads = queries.shape[1] // HEAD_DIM
    group_size = heads // kv_count
    q2 = queries.reshape(rows_here * heads, HEAD_DIM)
    grid_spec = pltpu.PrefetchScalarGridSpec(
        num_scalar_prefetch=1,
        grid=(rows_here, kv_count),
        in_specs=[
            pl.BlockSpec((group_size, HEAD_DIM), lambda i, k, n: (i * kv_count + k, 0)),
            pl.BlockSpec((1, span, HEAD_DIM), lambda i, k, n: (i, 0, k)),
            pl.BlockSpec((1, span, HEAD_DIM), lambda i, k, n: (i, 0, k)),
        ],
        out_specs=pl.BlockSpec((group_size, HEAD_DIM), lambda i, k, n: (i * kv_count + k, 0)),
    )
    return pl.pallas_call(
        attend_kernel,
        grid_spec=grid_spec,
        out_shape=jax.ShapeDtypeStruct((rows_here * heads, HEAD_DIM), jnp.bfloat16),
    )(lengths, q2, keys, values)


ROWS = ("chip", "core")


def pick(pair, first):
    return jnp.where(lax.axis_index("core") == first, pair[0], pair[1])


def gather_rows(x, chips):
    halves = x.reshape(2 * x.shape[0], x.shape[1] // 2)
    copies = jnp.broadcast_to(halves[None], (chips,) + halves.shape).reshape((chips * halves.shape[0], halves.shape[1]))
    mine = lax.all_to_all(copies, "chip", split_axis=0, concat_axis=0, tiled=True)
    mine = mine.reshape(chips, x.shape[0], x.shape[1])
    mate = lax.ppermute(mine, "core", [(0, 1), (1, 0)])
    first = pick((mine, mate), 0)
    second = pick((mate, mine), 0)
    return jnp.stack([first, second], axis=1).reshape(chips * 2 * x.shape[0], x.shape[1])


def scatter_rows(x, chips, narrow=False):
    per = x.shape[0] // (2 * chips)
    split = x.reshape(chips, 2, per, x.shape[1])
    keep = pick((split[:, 0], split[:, 1]), 0)
    give = pick((split[:, 1], split[:, 0]), 0)
    summed = keep + lax.ppermute(give, "core", [(0, 1), (1, 0)])
    if narrow:
        sent = summed.astype(jnp.bfloat16).reshape(chips * per * 2, x.shape[1] // 2)
        got = lax.all_to_all(sent, "chip", split_axis=0, concat_axis=0, tiled=True)
        return got.astype(jnp.float32).reshape(chips, per, x.shape[1]).sum(axis=0)
    got = lax.all_to_all(summed.reshape(chips * per, x.shape[1]), "chip", split_axis=0, concat_axis=0, tiled=True)
    return got.reshape(chips, per, x.shape[1]).sum(axis=0)


def shards(
    queries,
    keys,
    values,
    lengths,
    resid,
    out_weight,
    chat_ids,
    enc_weight,
    enc_bias,
    dec_weight,
    dec_bias,
):
    chips = lax.axis_size("chip")
    rows_here = queries.shape[0]
    key_width = keys.shape[2]
    kv_count = key_width // HEAD_DIM
    heads = queries.shape[1] // HEAD_DIM
    group_size = heads // kv_count
    attended = attend(queries, keys, values, lengths)
    count = 2 * chips
    if heads % count == 0:
        blocks = attended.reshape(rows_here * count, heads // count, HEAD_DIM)
        got = lax.all_to_all(blocks, ROWS, split_axis=0, concat_axis=0, tiled=True)
        features = got.reshape(count * rows_here, (heads // count) * HEAD_DIM)
    else:
        attended = attended.reshape(rows_here, heads * HEAD_DIM)
        features = lax.all_to_all(attended, ROWS, split_axis=1, concat_axis=0, tiled=True)
    partial_value = jnp.dot(features, out_weight, preferred_element_type=jnp.float32)
    hidden_here = (scatter_rows(partial_value, chips, narrow=True) + resid.astype(jnp.float32)).astype(jnp.bfloat16)
    hidden = gather_rows(hidden_here, chips)
    lat_here = enc_weight.shape[1]
    latent_ids = lax.axis_index(ROWS) * lat_here + lax.broadcasted_iota(jnp.int32, (lat_here,), 0)
    listed = jnp.any(chat_ids[:, None] == latent_ids[None, :], axis=0)
    activity = jnp.where(
        listed[None, :],
        0.0,
        jax.nn.relu(
            jnp.dot(hidden, enc_weight, preferred_element_type=jnp.float32) + enc_bias[None, :]
        ),
    ).astype(jnp.bfloat16)
    rebuilt = scatter_rows(jnp.dot(activity, dec_weight, preferred_element_type=jnp.float32), chips, narrow=True)
    spliced = (rebuilt + dec_bias[None, :]).astype(jnp.bfloat16)
    return (spliced, activity)


def solution(mesh):
    groups, count = mesh.devices.shape
    paired = Mesh(mesh.devices.reshape(groups, count // 2, 2), ("groups",) + ROWS)
    lead = ("groups",) + ROWS
    placed = (
        P(lead, None),
        P(lead, None, None),
        P(lead, None, None),
        P(lead),
        P(lead, None),
        P(ROWS, None),
        P(),
        P(None, ROWS),
        P(ROWS),
        P(ROWS, None),
        P(),
    )
    return jax.shard_map(
        shards,
        mesh=paired,
        in_specs=placed,
        out_specs=(P(lead, None), P("groups", ROWS)),
        check_vma=False,
    )
```

```python
import jax
import jax.numpy as jnp
from jax import lax
from jax.sharding import Mesh, PartitionSpec as P

HEAD_DIM = 128


ROWS = ("chip", "core")


def pick(pair, first):
    return jnp.where(lax.axis_index("core") == first, pair[0], pair[1])


def gather_rows(x, chips):
    halves = x.reshape(2 * x.shape[0], x.shape[1] // 2)
    copies = jnp.broadcast_to(halves[None], (chips,) + halves.shape).reshape((chips * halves.shape[0], halves.shape[1]))
    mine = lax.all_to_all(copies, "chip", split_axis=0, concat_axis=0, tiled=True)
    mine = mine.reshape(chips, x.shape[0], x.shape[1])
    mate = lax.ppermute(mine, "core", [(0, 1), (1, 0)])
    first = pick((mine, mate), 0)
    second = pick((mate, mine), 0)
    return jnp.stack([first, second], axis=1).reshape(chips * 2 * x.shape[0], x.shape[1])


def reduce_gather_rows(x, resid, chips):
    per = x.shape[0] // (2 * chips)
    width = x.shape[1]
    split = x.reshape(chips, 2, per, width)
    keep = pick((split[:, 0], split[:, 1]), 0)
    give = pick((split[:, 1], split[:, 0]), 0)
    summed = keep + lax.ppermute(give, "core", [(0, 1), (1, 0)])
    payload = jnp.concatenate([summed.astype(jnp.bfloat16).reshape(chips * per, width), resid], axis=0)
    halves = payload.reshape(2 * (chips + 1) * per, width // 2)
    copies = jnp.broadcast_to(halves[None], (chips,) + halves.shape).reshape(chips * halves.shape[0], width // 2)
    got = lax.all_to_all(copies, "chip", split_axis=0, concat_axis=0, tiled=True)
    got = got.reshape(chips, chips + 1, per, width).astype(jnp.float32)
    mine = (got[:, :chips].sum(axis=0) + got[:, chips]).astype(jnp.bfloat16)
    mate = lax.ppermute(mine, "core", [(0, 1), (1, 0)])
    first = pick((mine, mate), 0)
    second = pick((mate, mine), 0)
    return jnp.stack([first, second], axis=1).reshape(chips * 2 * per, width)


def scatter_rows(x, chips, narrow=False):
    per = x.shape[0] // (2 * chips)
    split = x.reshape(chips, 2, per, x.shape[1])
    keep = pick((split[:, 0], split[:, 1]), 0)
    give = pick((split[:, 1], split[:, 0]), 0)
    summed = keep + lax.ppermute(give, "core", [(0, 1), (1, 0)])
    if narrow:
        sent = summed.astype(jnp.bfloat16).reshape(chips * per * 2, x.shape[1] // 2)
        got = lax.all_to_all(sent, "chip", split_axis=0, concat_axis=0, tiled=True)
        return got.astype(jnp.float32).reshape(chips, per, x.shape[1]).sum(axis=0)
    got = lax.all_to_all(summed.reshape(chips * per, x.shape[1]), "chip", split_axis=0, concat_axis=0, tiled=True)
    return got.reshape(chips, per, x.shape[1]).sum(axis=0)


def shards(
    queries,
    keys,
    values,
    lengths,
    resid,
    out_weight,
    chat_ids,
    enc_weight,
    enc_bias,
    dec_weight,
    dec_bias,
):
    chips = lax.axis_size("chip")
    rows_here = queries.shape[0]
    key_width = keys.shape[2]
    kv_count = key_width // HEAD_DIM
    heads = queries.shape[1] // HEAD_DIM
    group_size = heads // kv_count
    head_of = lax.broadcasted_iota(jnp.int32, (heads, kv_count), 0) // group_size
    block_of = lax.broadcasted_iota(jnp.int32, (heads, kv_count), 1)
    onehot = (head_of == block_of).astype(jnp.bfloat16)
    query_heads = queries.reshape(rows_here, heads, 1, HEAD_DIM)
    spread = (query_heads * onehot[None, :, :, None]).reshape(rows_here, heads, key_width)
    scores = jnp.einsum("rhc,rsc->rhs", spread, keys, preferred_element_type=jnp.float32)
    scores = scores / jnp.sqrt(jnp.float32(HEAD_DIM))
    cache_span = keys.shape[1]
    visible = lax.broadcasted_iota(jnp.int32, (rows_here, cache_span), 1) < lengths[:, None]
    scores = jnp.where(visible[:, None, :], scores, -jnp.inf)
    highest = jnp.max(scores, axis=-1, keepdims=True)
    expo = jnp.exp(scores - highest)
    weights = (expo / jnp.sum(expo, axis=-1, keepdims=True)).astype(jnp.bfloat16)
    mixed = jnp.einsum("rhs,rsc->rhc", weights, values, preferred_element_type=jnp.float32)
    mixed = lax.optimization_barrier(mixed).reshape(rows_here, heads, kv_count, HEAD_DIM) * onehot.astype(jnp.float32)[None, :, :, None]
    attended = mixed.sum(axis=2).astype(jnp.bfloat16)
    count = 2 * chips
    if heads % count == 0:
        blocks = attended.reshape(rows_here * count, heads // count, HEAD_DIM)
        got = lax.all_to_all(blocks, ROWS, split_axis=0, concat_axis=0, tiled=True)
        features = got.reshape(count * rows_here, (heads // count) * HEAD_DIM)
    else:
        attended = attended.reshape(rows_here, heads * HEAD_DIM)
        features = lax.all_to_all(attended, ROWS, split_axis=1, concat_axis=0, tiled=True)
    partial_value = jnp.dot(features, out_weight, preferred_element_type=jnp.float32)
    if chips <= 8:
        hidden = reduce_gather_rows(partial_value, resid, chips)
    else:
        hidden_here = (scatter_rows(partial_value, chips, narrow=True) + resid.astype(jnp.float32)).astype(jnp.bfloat16)
        hidden = gather_rows(hidden_here, chips)
    lat_here = enc_weight.shape[1]
    latent_ids = lax.axis_index(ROWS) * lat_here + lax.broadcasted_iota(jnp.int32, (lat_here,), 0)
    listed = jnp.any(chat_ids[:, None] == latent_ids[None, :], axis=0)
    activity = jnp.where(
        listed[None, :],
        0.0,
        jax.nn.relu(
            jnp.dot(hidden, enc_weight, preferred_element_type=jnp.float32) + enc_bias[None, :]
        ),
    ).astype(jnp.bfloat16)
    rebuilt = scatter_rows(jnp.dot(activity, dec_weight, preferred_element_type=jnp.float32), chips, narrow=True)
    spliced = (rebuilt + dec_bias[None, :]).astype(jnp.bfloat16)
    return (spliced, activity)


def solution(mesh):
    groups, count = mesh.devices.shape
    paired = Mesh(mesh.devices.reshape(groups, count // 2, 2), ("groups",) + ROWS)
    lead = ("groups",) + ROWS
    placed = (
        P(lead, None),
        P(lead, None, None),
        P(lead, None, None),
        P(lead),
        P(lead, None),
        P(ROWS, None),
        P(),
        P(None, ROWS),
        P(ROWS),
        P(ROWS, None),
        P(),
    )
    return jax.shard_map(
        shards,
        mesh=paired,
        in_specs=placed,
        out_specs=(P(lead, None), P("groups", ROWS)),
        check_vma=False,
    )
```

```python
import jax
import jax.numpy as jnp
from jax import lax
from jax.sharding import Mesh, PartitionSpec as P

HEAD_DIM = 128


ROWS = ("chip", "core")


def pick(pair, first):
    return jnp.where(lax.axis_index("core") == first, pair[0], pair[1])


def gather_rows(x, chips):
    halves = x.reshape(2 * x.shape[0], x.shape[1] // 2)
    copies = jnp.broadcast_to(halves[None], (chips,) + halves.shape).reshape((chips * halves.shape[0], halves.shape[1]))
    mine = lax.all_to_all(copies, "chip", split_axis=0, concat_axis=0, tiled=True)
    mine = mine.reshape(chips, x.shape[0], x.shape[1])
    mate = lax.ppermute(mine, "core", [(0, 1), (1, 0)])
    first = pick((mine, mate), 0)
    second = pick((mate, mine), 0)
    return jnp.stack([first, second], axis=1).reshape(chips * 2 * x.shape[0], x.shape[1])


def scatter_rows(lhs, weight, chips):
    per = lhs.shape[0] // (2 * chips)
    split = lhs.reshape(chips, 2, per, lhs.shape[1])
    keep = pick((split[:, 0], split[:, 1]), 0).reshape(chips * per, lhs.shape[1])
    give = pick((split[:, 1], split[:, 0]), 0).reshape(chips * per, lhs.shape[1])
    sent_over = lax.ppermute(
        jnp.dot(give, weight, preferred_element_type=jnp.float32), "core", [(0, 1), (1, 0)]
    )
    summed = lax.optimization_barrier(jnp.dot(keep, weight, preferred_element_type=jnp.float32)) + sent_over
    width = weight.shape[1]
    sent = summed.astype(jnp.bfloat16).reshape(chips * per * 2, width // 2)
    got = lax.all_to_all(sent, "chip", split_axis=0, concat_axis=0, tiled=True)
    return got.astype(jnp.float32).reshape(chips, per, width).sum(axis=0)


def shards(
    queries,
    keys,
    values,
    lengths,
    resid,
    out_weight,
    chat_ids,
    enc_weight,
    enc_bias,
    dec_weight,
    dec_bias,
):
    chips = lax.axis_size("chip")
    rows_here = queries.shape[0]
    key_width = keys.shape[2]
    kv_count = key_width // HEAD_DIM
    heads = queries.shape[1] // HEAD_DIM
    group_size = heads // kv_count
    head_of = lax.broadcasted_iota(jnp.int32, (heads, kv_count), 0) // group_size
    block_of = lax.broadcasted_iota(jnp.int32, (heads, kv_count), 1)
    onehot = (head_of == block_of).astype(jnp.bfloat16)
    query_heads = queries.reshape(rows_here, heads, 1, HEAD_DIM)
    spread = (query_heads * onehot[None, :, :, None]).reshape(rows_here, heads, key_width)
    scores = jnp.einsum("rhc,rsc->rhs", spread, keys, preferred_element_type=jnp.float32)
    scores = scores / jnp.sqrt(jnp.float32(HEAD_DIM))
    cache_span = keys.shape[1]
    visible = lax.broadcasted_iota(jnp.int32, (rows_here, cache_span), 1) < lengths[:, None]
    scores = jnp.where(visible[:, None, :], scores, -jnp.inf)
    highest = jnp.max(scores, axis=-1, keepdims=True)
    expo = jnp.exp(scores - highest)
    weights = (expo / jnp.sum(expo, axis=-1, keepdims=True)).astype(jnp.bfloat16)
    mixed = jnp.einsum("rhs,rsc->rhc", weights, values, preferred_element_type=jnp.float32)
    mixed = lax.optimization_barrier(mixed).reshape(rows_here, heads, kv_count, HEAD_DIM) * onehot.astype(jnp.float32)[None, :, :, None]
    attended = mixed.sum(axis=2).astype(jnp.bfloat16)
    count = 2 * chips
    if heads % count == 0:
        blocks = attended.reshape(rows_here * count, heads // count, HEAD_DIM)
        got = lax.all_to_all(blocks, ROWS, split_axis=0, concat_axis=0, tiled=True)
        features = got.reshape(count * rows_here, (heads // count) * HEAD_DIM)
    else:
        attended = attended.reshape(rows_here, heads * HEAD_DIM)
        features = lax.all_to_all(attended, ROWS, split_axis=1, concat_axis=0, tiled=True)
    hidden_here = (scatter_rows(features, out_weight, chips) + resid.astype(jnp.float32)).astype(jnp.bfloat16)
    hidden = gather_rows(hidden_here, chips)
    lat_here = enc_weight.shape[1]
    latent_ids = lax.axis_index(ROWS) * lat_here + lax.broadcasted_iota(jnp.int32, (lat_here,), 0)
    listed = jnp.any(chat_ids[:, None] == latent_ids[None, :], axis=0)
    activity = jnp.where(
        listed[None, :],
        0.0,
        jax.nn.relu(
            jnp.dot(hidden, enc_weight, preferred_element_type=jnp.float32) + enc_bias[None, :]
        ),
    ).astype(jnp.bfloat16)
    rebuilt = scatter_rows(activity, dec_weight, chips)
    spliced = (rebuilt + dec_bias[None, :]).astype(jnp.bfloat16)
    return (spliced, activity)


def solution(mesh):
    groups, count = mesh.devices.shape
    paired = Mesh(mesh.devices.reshape(groups, count // 2, 2), ("groups",) + ROWS)
    lead = ("groups",) + ROWS
    placed = (
        P(lead, None),
        P(lead, None, None),
        P(lead, None, None),
        P(lead),
        P(lead, None),
        P(ROWS, None),
        P(),
        P(None, ROWS),
        P(ROWS),
        P(ROWS, None),
        P(),
    )
    return jax.shard_map(
        shards,
        mesh=paired,
        in_specs=placed,
        out_specs=(P(lead, None), P("groups", ROWS)),
        check_vma=False,
    )
```

```python
import jax
import jax.numpy as jnp
from jax import lax
from jax.sharding import Mesh, PartitionSpec as P

HEAD_DIM = 128


ROWS = ("chip", "core")


def pick(pair, first):
    return jnp.where(lax.axis_index("core") == first, pair[0], pair[1])


def gather_rows(x, chips):
    halves = x.reshape(2 * x.shape[0], x.shape[1] // 2)
    copies = jnp.broadcast_to(halves[None], (chips,) + halves.shape).reshape((chips * halves.shape[0], halves.shape[1]))
    mine = lax.all_to_all(copies, "chip", split_axis=0, concat_axis=0, tiled=True)
    mine = mine.reshape(chips, x.shape[0], x.shape[1])
    mate = lax.ppermute(mine, "core", [(0, 1), (1, 0)])
    first = pick((mine, mate), 0)
    second = pick((mate, mine), 0)
    return jnp.stack([first, second], axis=1).reshape(chips * 2 * x.shape[0], x.shape[1])


def gather_all_rows(x, count):
    halves = x.reshape(2 * x.shape[0], x.shape[1] // 2)
    copies = jnp.broadcast_to(halves[None], (count,) + halves.shape).reshape((count * halves.shape[0], halves.shape[1]))
    got = lax.all_to_all(copies, ROWS, split_axis=0, concat_axis=0, tiled=True)
    return got.reshape(count * x.shape[0], x.shape[1])


def scatter_rows(x, chips, narrow=False):
    per = x.shape[0] // (2 * chips)
    split = x.reshape(chips, 2, per, x.shape[1])
    keep = pick((split[:, 0], split[:, 1]), 0)
    give = pick((split[:, 1], split[:, 0]), 0)
    summed = keep + lax.ppermute(give, "core", [(0, 1), (1, 0)])
    if narrow:
        sent = summed.astype(jnp.bfloat16).reshape(chips * per * 2, x.shape[1] // 2)
        got = lax.all_to_all(sent, "chip", split_axis=0, concat_axis=0, tiled=True)
        return got.astype(jnp.float32).reshape(chips, per, x.shape[1]).sum(axis=0)
    got = lax.all_to_all(summed.reshape(chips * per, x.shape[1]), "chip", split_axis=0, concat_axis=0, tiled=True)
    return got.reshape(chips, per, x.shape[1]).sum(axis=0)


def shards(
    queries,
    keys,
    values,
    lengths,
    resid,
    out_weight,
    chat_ids,
    enc_weight,
    enc_bias,
    dec_weight,
    dec_bias,
):
    chips = lax.axis_size("chip")
    rows_here = queries.shape[0]
    key_width = keys.shape[2]
    kv_count = key_width // HEAD_DIM
    heads = queries.shape[1] // HEAD_DIM
    group_size = heads // kv_count
    head_of = lax.broadcasted_iota(jnp.int32, (heads, kv_count), 0) // group_size
    block_of = lax.broadcasted_iota(jnp.int32, (heads, kv_count), 1)
    onehot = (head_of == block_of).astype(jnp.bfloat16)
    query_heads = queries.reshape(rows_here, heads, 1, HEAD_DIM)
    spread = (query_heads * onehot[None, :, :, None]).reshape(rows_here, heads, key_width)
    scores = jnp.einsum("rhc,rsc->rhs", spread, keys, preferred_element_type=jnp.float32)
    scores = scores / jnp.sqrt(jnp.float32(HEAD_DIM))
    cache_span = keys.shape[1]
    visible = lax.broadcasted_iota(jnp.int32, (rows_here, cache_span), 1) < lengths[:, None]
    scores = jnp.where(visible[:, None, :], scores, -jnp.inf)
    highest = jnp.max(scores, axis=-1, keepdims=True)
    expo = jnp.exp(scores - highest)
    weights = (expo / jnp.sum(expo, axis=-1, keepdims=True)).astype(jnp.bfloat16)
    mixed = jnp.einsum("rhs,rsc->rhc", weights, values, preferred_element_type=jnp.float32)
    mixed = lax.optimization_barrier(mixed).reshape(rows_here, heads, kv_count, HEAD_DIM) * onehot.astype(jnp.float32)[None, :, :, None]
    attended = mixed.sum(axis=2).astype(jnp.bfloat16)
    count = 2 * chips
    if heads % count == 0:
        blocks = attended.reshape(rows_here * count, heads // count, HEAD_DIM)
        got = lax.all_to_all(blocks, ROWS, split_axis=0, concat_axis=0, tiled=True)
        features = got.reshape(count * rows_here, (heads // count) * HEAD_DIM)
    else:
        attended = attended.reshape(rows_here, heads * HEAD_DIM)
        features = lax.all_to_all(attended, ROWS, split_axis=1, concat_axis=0, tiled=True)
    partial_value = jnp.dot(features, out_weight, preferred_element_type=jnp.float32)
    hidden_here = (scatter_rows(partial_value, chips, narrow=True) + resid.astype(jnp.float32)).astype(jnp.bfloat16)
    hidden = gather_all_rows(hidden_here, 2 * chips)
    lat_here = enc_weight.shape[1]
    latent_ids = lax.axis_index(ROWS) * lat_here + lax.broadcasted_iota(jnp.int32, (lat_here,), 0)
    listed = jnp.any(chat_ids[:, None] == latent_ids[None, :], axis=0)
    activity = jnp.where(
        listed[None, :],
        0.0,
        jax.nn.relu(
            jnp.dot(hidden, enc_weight, preferred_element_type=jnp.float32) + enc_bias[None, :]
        ),
    ).astype(jnp.bfloat16)
    rebuilt = scatter_rows(jnp.dot(activity, dec_weight, preferred_element_type=jnp.float32), chips, narrow=True)
    spliced = (rebuilt + dec_bias[None, :]).astype(jnp.bfloat16)
    return (spliced, activity)


def solution(mesh):
    groups, count = mesh.devices.shape
    paired = Mesh(mesh.devices.reshape(groups, count // 2, 2), ("groups",) + ROWS)
    lead = ("groups",) + ROWS
    placed = (
        P(lead, None),
        P(lead, None, None),
        P(lead, None, None),
        P(lead),
        P(lead, None),
        P(ROWS, None),
        P(),
        P(None, ROWS),
        P(ROWS),
        P(ROWS, None),
        P(),
    )
    return jax.shard_map(
        shards,
        mesh=paired,
        in_specs=placed,
        out_specs=(P(lead, None), P("groups", ROWS)),
        check_vma=False,
    )
```

```python
import jax
import jax.numpy as jnp
from jax import lax
from jax.sharding import Mesh, PartitionSpec as P

HEAD_DIM = 128


ROWS = ("chip", "core")


def pick(pair, first):
    return jnp.where(lax.axis_index("core") == first, pair[0], pair[1])


def gather_rows(x, chips):
    halves = x.reshape(2 * x.shape[0], x.shape[1] // 2)
    copies = jnp.broadcast_to(halves[None], (chips,) + halves.shape).reshape((chips * halves.shape[0], halves.shape[1]))
    mine = lax.all_to_all(copies, "chip", split_axis=0, concat_axis=0, tiled=True)
    mine = mine.reshape(chips, x.shape[0], x.shape[1])
    mate = lax.ppermute(mine, "core", [(0, 1), (1, 0)])
    first = pick((mine, mate), 0)
    second = pick((mate, mine), 0)
    return jnp.stack([first, second], axis=1).reshape(chips * 2 * x.shape[0], x.shape[1])


def gather_all_rows(x, count):
    halves = x.reshape(2 * x.shape[0], x.shape[1] // 2)
    copies = jnp.broadcast_to(halves[None], (count,) + halves.shape).reshape((count * halves.shape[0], halves.shape[1]))
    got = lax.all_to_all(copies, ROWS, split_axis=0, concat_axis=0, tiled=True)
    return got.reshape(count * x.shape[0], x.shape[1])


def scatter_all_rows(x, count):
    per = x.shape[0] // count
    sent = x.astype(jnp.bfloat16).reshape(count * per * 2, x.shape[1] // 2)
    got = lax.all_to_all(sent, ROWS, split_axis=0, concat_axis=0, tiled=True)
    return got.astype(jnp.float32).reshape(count, per, x.shape[1]).sum(axis=0)


def scatter_rows(x, chips, narrow=False):
    per = x.shape[0] // (2 * chips)
    split = x.reshape(chips, 2, per, x.shape[1])
    keep = pick((split[:, 0], split[:, 1]), 0)
    give = pick((split[:, 1], split[:, 0]), 0)
    summed = keep + lax.ppermute(give, "core", [(0, 1), (1, 0)])
    if narrow:
        sent = summed.astype(jnp.bfloat16).reshape(chips * per * 2, x.shape[1] // 2)
        got = lax.all_to_all(sent, "chip", split_axis=0, concat_axis=0, tiled=True)
        return got.astype(jnp.float32).reshape(chips, per, x.shape[1]).sum(axis=0)
    got = lax.all_to_all(summed.reshape(chips * per, x.shape[1]), "chip", split_axis=0, concat_axis=0, tiled=True)
    return got.reshape(chips, per, x.shape[1]).sum(axis=0)


def shards(
    queries,
    keys,
    values,
    lengths,
    resid,
    out_weight,
    chat_ids,
    enc_weight,
    enc_bias,
    dec_weight,
    dec_bias,
):
    chips = lax.axis_size("chip")
    rows_here = queries.shape[0]
    key_width = keys.shape[2]
    kv_count = key_width // HEAD_DIM
    heads = queries.shape[1] // HEAD_DIM
    group_size = heads // kv_count
    head_of = lax.broadcasted_iota(jnp.int32, (heads, kv_count), 0) // group_size
    block_of = lax.broadcasted_iota(jnp.int32, (heads, kv_count), 1)
    onehot = (head_of == block_of).astype(jnp.bfloat16)
    query_heads = queries.reshape(rows_here, heads, 1, HEAD_DIM)
    spread = (query_heads * onehot[None, :, :, None]).reshape(rows_here, heads, key_width)
    scores = jnp.einsum("rhc,rsc->rhs", spread, keys, preferred_element_type=jnp.float32)
    scores = scores / jnp.sqrt(jnp.float32(HEAD_DIM))
    cache_span = keys.shape[1]
    visible = lax.broadcasted_iota(jnp.int32, (rows_here, cache_span), 1) < lengths[:, None]
    scores = jnp.where(visible[:, None, :], scores, -jnp.inf)
    highest = jnp.max(scores, axis=-1, keepdims=True)
    expo = jnp.exp(scores - highest)
    weights = (expo / jnp.sum(expo, axis=-1, keepdims=True)).astype(jnp.bfloat16)
    mixed = jnp.einsum("rhs,rsc->rhc", weights, values, preferred_element_type=jnp.float32)
    mixed = lax.optimization_barrier(mixed).reshape(rows_here, heads, kv_count, HEAD_DIM) * onehot.astype(jnp.float32)[None, :, :, None]
    attended = mixed.sum(axis=2).astype(jnp.bfloat16)
    count = 2 * chips
    if heads % count == 0:
        blocks = attended.reshape(rows_here * count, heads // count, HEAD_DIM)
        got = lax.all_to_all(blocks, ROWS, split_axis=0, concat_axis=0, tiled=True)
        features = got.reshape(count * rows_here, (heads // count) * HEAD_DIM)
    else:
        attended = attended.reshape(rows_here, heads * HEAD_DIM)
        features = lax.all_to_all(attended, ROWS, split_axis=1, concat_axis=0, tiled=True)
    partial_value = jnp.dot(features, out_weight, preferred_element_type=jnp.float32)
    hidden_here = (scatter_all_rows(partial_value, 2 * chips) + resid.astype(jnp.float32)).astype(jnp.bfloat16)
    hidden = gather_all_rows(hidden_here, 2 * chips)
    lat_here = enc_weight.shape[1]
    latent_ids = lax.axis_index(ROWS) * lat_here + lax.broadcasted_iota(jnp.int32, (lat_here,), 0)
    listed = jnp.any(chat_ids[:, None] == latent_ids[None, :], axis=0)
    activity = jnp.where(
        listed[None, :],
        0.0,
        jax.nn.relu(
            jnp.dot(hidden, enc_weight, preferred_element_type=jnp.float32) + enc_bias[None, :]
        ),
    ).astype(jnp.bfloat16)
    rebuilt = scatter_all_rows(jnp.dot(activity, dec_weight, preferred_element_type=jnp.float32), 2 * chips)
    spliced = (rebuilt + dec_bias[None, :]).astype(jnp.bfloat16)
    return (spliced, activity)


def solution(mesh):
    groups, count = mesh.devices.shape
    paired = Mesh(mesh.devices.reshape(groups, count // 2, 2), ("groups",) + ROWS)
    lead = ("groups",) + ROWS
    placed = (
        P(lead, None),
        P(lead, None, None),
        P(lead, None, None),
        P(lead),
        P(lead, None),
        P(ROWS, None),
        P(),
        P(None, ROWS),
        P(ROWS),
        P(ROWS, None),
        P(),
    )
    return jax.shard_map(
        shards,
        mesh=paired,
        in_specs=placed,
        out_specs=(P(lead, None), P("groups", ROWS)),
        check_vma=False,
    )
```

```python
import jax
import jax.numpy as jnp
from jax import lax
from jax.sharding import Mesh, PartitionSpec as P

HEAD_DIM = 128


ROWS = ("chip", "core")


def pick(pair, first):
    return jnp.where(lax.axis_index("core") == first, pair[0], pair[1])


def gather_rows(x, chips):
    halves = x.reshape(2 * x.shape[0], x.shape[1] // 2)
    copies = jnp.broadcast_to(halves[None], (chips,) + halves.shape).reshape((chips * halves.shape[0], halves.shape[1]))
    mine = lax.all_to_all(copies, "chip", split_axis=0, concat_axis=0, tiled=True)
    mine = mine.reshape(chips, x.shape[0], x.shape[1])
    mate = lax.ppermute(mine, "core", [(0, 1), (1, 0)])
    first = pick((mine, mate), 0)
    second = pick((mate, mine), 0)
    return jnp.stack([first, second], axis=1).reshape(chips * 2 * x.shape[0], x.shape[1])


def gather_all_rows(x, count):
    halves = x.reshape(2 * x.shape[0], x.shape[1] // 2)
    copies = jnp.broadcast_to(halves[None], (count,) + halves.shape).reshape((count * halves.shape[0], halves.shape[1]))
    got = lax.all_to_all(copies, ROWS, split_axis=0, concat_axis=0, tiled=True)
    return got.reshape(count * x.shape[0], x.shape[1])


def scatter_all_rows(x, count):
    per = x.shape[0] // count
    sent = x.astype(jnp.bfloat16).reshape(count * per * 2, x.shape[1] // 2)
    got = lax.all_to_all(sent, ROWS, split_axis=0, concat_axis=0, tiled=True)
    return got.astype(jnp.float32).reshape(count, per, x.shape[1]).sum(axis=0)


def scatter_rows(x, chips, narrow=False):
    per = x.shape[0] // (2 * chips)
    split = x.reshape(chips, 2, per, x.shape[1])
    keep = pick((split[:, 0], split[:, 1]), 0)
    give = pick((split[:, 1], split[:, 0]), 0)
    summed = keep + lax.ppermute(give, "core", [(0, 1), (1, 0)])
    if narrow:
        sent = summed.astype(jnp.bfloat16).reshape(chips * per * 2, x.shape[1] // 2)
        got = lax.all_to_all(sent, "chip", split_axis=0, concat_axis=0, tiled=True)
        return got.astype(jnp.float32).reshape(chips, per, x.shape[1]).sum(axis=0)
    got = lax.all_to_all(summed.reshape(chips * per, x.shape[1]), "chip", split_axis=0, concat_axis=0, tiled=True)
    return got.reshape(chips, per, x.shape[1]).sum(axis=0)


def shards(
    queries,
    keys,
    values,
    lengths,
    resid,
    out_weight,
    chat_ids,
    enc_weight,
    enc_bias,
    dec_weight,
    dec_bias,
):
    chips = lax.axis_size("chip")
    rows_here = queries.shape[0]
    key_width = keys.shape[2]
    kv_count = key_width // HEAD_DIM
    heads = queries.shape[1] // HEAD_DIM
    group_size = heads // kv_count
    head_of = lax.broadcasted_iota(jnp.int32, (heads, kv_count), 0) // group_size
    block_of = lax.broadcasted_iota(jnp.int32, (heads, kv_count), 1)
    onehot = (head_of == block_of).astype(jnp.bfloat16)
    query_heads = queries.reshape(rows_here, heads, 1, HEAD_DIM)
    spread = (query_heads * onehot[None, :, :, None]).reshape(rows_here, heads, key_width)
    scores = jnp.einsum("rhc,rsc->rhs", spread, keys, preferred_element_type=jnp.float32)
    scores = scores / jnp.sqrt(jnp.float32(HEAD_DIM))
    cache_span = keys.shape[1]
    visible = lax.broadcasted_iota(jnp.float32, (rows_here, cache_span), 1) < lengths.astype(jnp.float32)[:, None]
    scores = jnp.where(visible[:, None, :], scores, -jnp.inf)
    highest = jnp.max(scores, axis=-1, keepdims=True)
    expo = jnp.exp(scores - highest)
    weights = (expo / jnp.sum(expo, axis=-1, keepdims=True)).astype(jnp.bfloat16)
    mixed = jnp.einsum("rhs,rsc->rhc", weights, values, preferred_element_type=jnp.float32)
    mixed = lax.optimization_barrier(mixed).reshape(rows_here, heads, kv_count, HEAD_DIM) * onehot.astype(jnp.float32)[None, :, :, None]
    attended = mixed.sum(axis=2).astype(jnp.bfloat16)
    count = 2 * chips
    if heads % count == 0:
        blocks = attended.reshape(rows_here * count, heads // count, HEAD_DIM)
        got = lax.all_to_all(blocks, ROWS, split_axis=0, concat_axis=0, tiled=True)
        features = got.reshape(count * rows_here, (heads // count) * HEAD_DIM)
    else:
        attended = attended.reshape(rows_here, heads * HEAD_DIM)
        features = lax.all_to_all(attended, ROWS, split_axis=1, concat_axis=0, tiled=True)
    partial_value = jnp.dot(features, out_weight, preferred_element_type=jnp.float32)
    hidden_here = (scatter_all_rows(partial_value, 2 * chips) + resid.astype(jnp.float32)).astype(jnp.bfloat16)
    hidden = gather_all_rows(hidden_here, 2 * chips)
    lat_here = enc_weight.shape[1]
    latent_ids = lax.axis_index(ROWS) * lat_here + lax.broadcasted_iota(jnp.int32, (lat_here,), 0)
    listed = jnp.any(chat_ids[:, None] == latent_ids[None, :], axis=0)
    activity = jnp.where(
        listed[None, :],
        0.0,
        jax.nn.relu(
            jnp.dot(hidden, enc_weight, preferred_element_type=jnp.float32) + enc_bias[None, :]
        ),
    ).astype(jnp.bfloat16)
    rebuilt = scatter_all_rows(jnp.dot(activity, dec_weight, preferred_element_type=jnp.float32), 2 * chips)
    spliced = (rebuilt + dec_bias[None, :]).astype(jnp.bfloat16)
    return (spliced, activity)


def solution(mesh):
    groups, count = mesh.devices.shape
    paired = Mesh(mesh.devices.reshape(groups, count // 2, 2), ("groups",) + ROWS)
    lead = ("groups",) + ROWS
    placed = (
        P(lead, None),
        P(lead, None, None),
        P(lead, None, None),
        P(lead),
        P(lead, None),
        P(ROWS, None),
        P(),
        P(None, ROWS),
        P(ROWS),
        P(ROWS, None),
        P(),
    )
    return jax.shard_map(
        shards,
        mesh=paired,
        in_specs=placed,
        out_specs=(P(lead, None), P("groups", ROWS)),
        check_vma=False,
    )
```

```python
import jax
import jax.numpy as jnp
from jax import lax
from jax.sharding import Mesh, PartitionSpec as P

HEAD_DIM = 128


ROWS = ("chip", "core")


def pick(pair, first):
    return jnp.where(lax.axis_index("core") == first, pair[0], pair[1])


def gather_rows(x, chips):
    halves = x.reshape(2 * x.shape[0], x.shape[1] // 2)
    copies = jnp.broadcast_to(halves[None], (chips,) + halves.shape).reshape((chips * halves.shape[0], halves.shape[1]))
    mine = lax.all_to_all(copies, "chip", split_axis=0, concat_axis=0, tiled=True)
    mine = mine.reshape(chips, x.shape[0], x.shape[1])
    mate = lax.ppermute(mine, "core", [(0, 1), (1, 0)])
    first = pick((mine, mate), 0)
    second = pick((mate, mine), 0)
    return jnp.stack([first, second], axis=1).reshape(chips * 2 * x.shape[0], x.shape[1])


def gather_all_rows(x, count):
    halves = x.reshape(2 * x.shape[0], x.shape[1] // 2)
    copies = jnp.broadcast_to(halves[None], (count,) + halves.shape).reshape((count * halves.shape[0], halves.shape[1]))
    got = lax.all_to_all(copies, ROWS, split_axis=0, concat_axis=0, tiled=True)
    return got.reshape(count * x.shape[0], x.shape[1])


def scatter_all_rows(x, count):
    per = x.shape[0] // count
    sent = x.astype(jnp.bfloat16).reshape(count * per * 2, x.shape[1] // 2)
    got = lax.all_to_all(sent, ROWS, split_axis=0, concat_axis=0, tiled=True)
    return got.astype(jnp.float32).reshape(count, per, x.shape[1]).sum(axis=0)


def scatter_rows(x, chips, narrow=False):
    per = x.shape[0] // (2 * chips)
    split = x.reshape(chips, 2, per, x.shape[1])
    keep = pick((split[:, 0], split[:, 1]), 0)
    give = pick((split[:, 1], split[:, 0]), 0)
    summed = keep + lax.ppermute(give, "core", [(0, 1), (1, 0)])
    if narrow:
        sent = summed.astype(jnp.bfloat16).reshape(chips * per * 2, x.shape[1] // 2)
        got = lax.all_to_all(sent, "chip", split_axis=0, concat_axis=0, tiled=True)
        return got.astype(jnp.float32).reshape(chips, per, x.shape[1]).sum(axis=0)
    got = lax.all_to_all(summed.reshape(chips * per, x.shape[1]), "chip", split_axis=0, concat_axis=0, tiled=True)
    return got.reshape(chips, per, x.shape[1]).sum(axis=0)


def shards(
    queries,
    keys,
    values,
    lengths,
    resid,
    out_weight,
    chat_ids,
    enc_weight,
    enc_bias,
    dec_weight,
    dec_bias,
):
    chips = lax.axis_size("chip")
    rows_here = queries.shape[0]
    key_width = keys.shape[2]
    kv_count = key_width // HEAD_DIM
    heads = queries.shape[1] // HEAD_DIM
    group_size = heads // kv_count
    head_of = lax.broadcasted_iota(jnp.int32, (heads, kv_count), 0) // group_size
    block_of = lax.broadcasted_iota(jnp.int32, (heads, kv_count), 1)
    onehot = (head_of == block_of).astype(jnp.bfloat16)
    query_heads = queries.reshape(rows_here, heads, 1, HEAD_DIM)
    spread = (query_heads * onehot[None, :, :, None]).reshape(rows_here, heads, key_width)
    scores = jnp.einsum("rhc,rsc->rhs", spread, keys, preferred_element_type=jnp.float32)
    scores = scores / jnp.sqrt(jnp.float32(HEAD_DIM))
    cache_span = keys.shape[1]
    visible = lax.broadcasted_iota(jnp.float32, (rows_here, cache_span), 1) < lengths.astype(jnp.float32)[:, None]
    scores = jnp.where(visible[:, None, :], scores, -jnp.inf)
    highest = jnp.max(scores, axis=-1, keepdims=True)
    expo = jnp.exp(scores - highest)
    weights = (expo / jnp.sum(expo, axis=-1, keepdims=True)).astype(jnp.bfloat16)
    mixed = jnp.einsum("rhs,rsc->rhc", weights, values, preferred_element_type=jnp.float32)
    mixed = lax.optimization_barrier(mixed).reshape(rows_here, heads, kv_count, HEAD_DIM) * onehot.astype(jnp.float32)[None, :, :, None]
    attended = mixed.sum(axis=2).astype(jnp.bfloat16)
    count = 2 * chips
    if heads % count == 0 and rows_here == 1:
        per = heads // count
        got = lax.all_to_all(attended.reshape(chips, 2 * per, HEAD_DIM), "chip", split_axis=0, concat_axis=0, tiled=True)
        got = got.reshape(chips, 2, per, HEAD_DIM)
        mine = pick((got[:, 0], got[:, 1]), 0)
        mate = lax.ppermute(pick((got[:, 1], got[:, 0]), 0), "core", [(0, 1), (1, 0)])
        first = pick((mine, mate), 0)
        second = pick((mate, mine), 0)
        features = jnp.stack([first, second], axis=1).reshape(count, per * HEAD_DIM)
    elif heads % count == 0:
        blocks = attended.reshape(rows_here * count, heads // count, HEAD_DIM)
        got = lax.all_to_all(blocks, ROWS, split_axis=0, concat_axis=0, tiled=True)
        features = got.reshape(count * rows_here, (heads // count) * HEAD_DIM)
    else:
        attended = attended.reshape(rows_here, heads * HEAD_DIM)
        features = lax.all_to_all(attended, ROWS, split_axis=1, concat_axis=0, tiled=True)
    partial_value = jnp.dot(features, out_weight, preferred_element_type=jnp.float32)
    hidden_here = (scatter_all_rows(partial_value, 2 * chips) + resid.astype(jnp.float32)).astype(jnp.bfloat16)
    hidden = gather_all_rows(hidden_here, 2 * chips)
    lat_here = enc_weight.shape[1]
    latent_ids = lax.axis_index(ROWS) * lat_here + lax.broadcasted_iota(jnp.int32, (lat_here,), 0)
    listed = jnp.any(chat_ids[:, None] == latent_ids[None, :], axis=0)
    activity = jnp.where(
        listed[None, :],
        0.0,
        jax.nn.relu(
            jnp.dot(hidden, enc_weight, preferred_element_type=jnp.float32) + enc_bias[None, :]
        ),
    ).astype(jnp.bfloat16)
    rebuilt = scatter_all_rows(jnp.dot(activity, dec_weight, preferred_element_type=jnp.float32), 2 * chips)
    spliced = (rebuilt + dec_bias[None, :]).astype(jnp.bfloat16)
    return (spliced, activity)


def solution(mesh):
    groups, count = mesh.devices.shape
    paired = Mesh(mesh.devices.reshape(groups, count // 2, 2), ("groups",) + ROWS)
    lead = ("groups",) + ROWS
    placed = (
        P(lead, None),
        P(lead, None, None),
        P(lead, None, None),
        P(lead),
        P(lead, None),
        P(ROWS, None),
        P(),
        P(None, ROWS),
        P(ROWS),
        P(ROWS, None),
        P(),
    )
    return jax.shard_map(
        shards,
        mesh=paired,
        in_specs=placed,
        out_specs=(P(lead, None), P("groups", ROWS)),
        check_vma=False,
    )
```
